128 devices in a mesh: sample: 32 (over x, y, core), protein: 4 (over z).
Axes of the slice: x: 4, y: 4, z: 4, core: 2. Of those that a mesh axis runs over, the one named last changes fastest.
Arguments:
- proteins: bfloat16 [16384, 2048], P('sample'), may hold values from -34 to 34
- dosage: bfloat16 [16384, 2048], P('sample'), may hold values from 0 to 2, as said below
Outputs:
- scores: float32 [2048, 2048], P('sample', 'protein')
The draws below stay inside these ranges and needn't reach their ends.
Inputs may be any that keep to these rules, and one draw needn't show every extreme that they name: `dosage`: allele dosages, whole numbers.
All inputs are finite; a program needn't handle non-finite values.
Results may differ from the reference program's by a relative error of at most 0.0003.
Values sent between devices are 32-bit elements; how exact they have to be, the bound alone decides.
No kernel may reach another device: no remote copies, remote signals or barrier semaphores. Data moves between devices by JAX's collectives and lax.ppermute only.
A program may use at most 128 MiB of HBM per device.

```python
import math
import jax
import jax.numpy as jnp
from jax import lax

PROTEINS = 2048
SAMPLES = 16384
VARIANTS = 2048


def draw_proteins(key, part):
    subkeys = jax.random.split(key, 3)
    independent = jnp.clip(jax.random.normal(subkeys[0], (SAMPLES, PROTEINS), jnp.float32), -6.0, 6.0)
    loadings = jnp.clip(0.3 * jax.random.normal(subkeys[2], (4, PROTEINS), jnp.float32), -1.2, 1.2)
    factors = jnp.clip(jax.random.normal(subkeys[1], (SAMPLES, 4), jnp.float32), -4.0, 4.0)
    summed = independent + factors[:, 0:1] * loadings[0:1, :]
    summed = summed + factors[:, 1:2] * loadings[1:2, :]
    summed = summed + factors[:, 2:3] * loadings[2:3, :]
    summed = summed + factors[:, 3:4] * loadings[3:4, :]
    return summed.astype(jnp.bfloat16)


def draw_dosage(key, part):
    subkeys = jax.random.split(key, 3)
    frequency = jax.random.randint(subkeys[0], (1, VARIANTS), 1, 16)
    stratum = 2 + jnp.arange(SAMPLES, dtype=jnp.int32)[:, None] * 8 // SAMPLES
    threshold = frequency * stratum
    first_allele = jax.random.randint(subkeys[1], (SAMPLES, VARIANTS), 0, 320) < threshold
    second_allele = jax.random.randint(subkeys[2], (SAMPLES, VARIANTS), 0, 320) < threshold
    counted = first_allele.astype(jnp.int32) + second_allele.astype(jnp.int32)
    return counted.astype(jnp.float32).astype(jnp.bfloat16)


def setup_inputs(seed: int = 0) -> dict:
    seeds = jax.random.split(jax.random.key(seed), 3)
    return {
        "proteins": draw_proteins(jax.random.fold_in(seeds[2], 71), 0),
        "dosage": draw_dosage(jax.random.fold_in(seeds[2], 71), 0),
    }


def right_solve(factor, rows):
    return jax.scipy.linalg.solve_triangular(factor, rows.T, lower=True).T

def reference(proteins, dosage):
    sample_count = proteins.shape[0]
    gram = jnp.dot(proteins.T.astype(jnp.float32), proteins.astype(jnp.float32), preferred_element_type=jnp.float32) / sample_count
    cross = jnp.dot(dosage.T.astype(jnp.float32), proteins.astype(jnp.float32), preferred_element_type=jnp.float32)
    protein_sums = lax.optimization_barrier(jnp.sum(proteins, axis=0, dtype=jnp.float32))
    dose_sums = lax.optimization_barrier(jnp.sum(dosage, axis=0, dtype=jnp.float32))
    dose_squares = lax.optimization_barrier(jnp.sum(dosage * dosage, axis=0, dtype=jnp.float32))
    means = dose_sums / sample_count
    spread = jnp.sqrt(dose_squares / sample_count - means * means + 1e-05)
    centred = (cross - means[:, None] * protein_sums[None, :]) / (spread[:, None] * math.sqrt(sample_count))
    factor = jnp.linalg.cholesky(gram)
    return right_solve(factor, centred)
```

```python
import functools
import math

import jax
import jax.numpy as jnp
from jax import lax
from jax.experimental import pallas as pl
from jax.experimental.pallas import tpu as pltpu
from jax.sharding import PartitionSpec as P

BLOCK = 128
CHUNK = 256
HIGHEST = lax.Precision.HIGHEST


def side_by_side(arrays, axis, dim, along):
    widths = [math.prod(a.shape[along:]) for a in arrays]
    both = jnp.concatenate(
        [a.reshape(*a.shape[:along], w) for a, w in zip(arrays, widths)], axis=along
    )
    filled = lax.psum_scatter(both, axis, scatter_dimension=dim, tiled=True)
    tiles = jnp.split(filled, [sum(widths[:k]) for k in range(1, len(widths))], axis=along)
    return tuple(
        (b.reshape(*filled.shape[:along], *a.shape[along:]) for a, b in zip(arrays, tiles))
    )


def dot_t(a, b):
    return lax.dot_general(
        a, b, (((1,), (1,)), ((), ())), precision=HIGHEST, preferred_element_type=jnp.float32
    )


def inverse_factor(block):
    b = block.shape[0]
    rio = lax.broadcasted_iota(jnp.int32, (b, b), 0)
    lio = lax.broadcasted_iota(jnp.int32, (b, b), 1)
    rcol = lax.broadcasted_iota(jnp.int32, (b, 1), 0)
    lrow = lax.broadcasted_iota(jnp.int32, (1, b), 1)

    def step(j, m):
        row = jnp.sum(jnp.where(rio == j, m, 0.0), axis=0, keepdims=True)
        pivot = jnp.sum(jnp.where(lrow == j, row, 0.0), axis=1, keepdims=True)
        scale = lax.rsqrt(pivot)
        new_row = jnp.where(lrow == j, scale, row * scale)
        col = jnp.sum(jnp.where(lio == j, m, 0.0), axis=1, keepdims=True)
        mult = jnp.where(rcol > j, col * scale, 0.0)
        m = jnp.where((rio > j) & (lio == j), 0.0, m) - mult * new_row
        return jnp.where(rio == j, jnp.where(lrow <= j, new_row, 0.0), m)

    return lax.fori_loop(0, b, step, block)


def factor_solve_kernel(g_hbm, c_ref, out_ref, g_ref, sem):
    n = g_ref.shape[0]
    b = BLOCK
    copy = pltpu.make_async_copy(g_hbm, g_ref, sem)
    copy.start()
    out_ref[...] = c_ref[...]
    copy.wait()
    for k in range(n // b):
        r0 = k * b
        inv = inverse_factor(g_ref[r0 : r0 + b, r0 : r0 + b])
        solved = dot_t(out_ref[:, r0 : r0 + b], inv)
        out_ref[:, r0 : r0 + b] = solved
        rest = r0 + b
        if rest < n:
            panel = dot_t(g_ref[rest:, r0 : r0 + b], inv)
            for a in range(rest, n, CHUNK):
                e = min(a + CHUNK, n)
                g_ref[a:e, rest:] = g_ref[a:e, rest:] - dot_t(panel[a - rest : e - rest], panel)
            out_ref[:, rest:] = out_ref[:, rest:] - dot_t(solved, panel)


def factor_solve(gram, rows):
    n = gram.shape[0]
    return pl.pallas_call(
        factor_solve_kernel,
        out_shape=jax.ShapeDtypeStruct(rows.shape, jnp.float32),
        in_specs=[
            pl.BlockSpec(memory_space=pl.ANY),
            pl.BlockSpec(memory_space=pltpu.VMEM),
        ],
        out_specs=pl.BlockSpec(memory_space=pltpu.VMEM),
        scratch_shapes=[pltpu.VMEM((n, n), jnp.float32), pltpu.SemaphoreType.DMA],
        compiler_params=pltpu.CompilerParams(vmem_limit_bytes=56 * 1024 * 1024),
    )(gram, rows)


def body(proteins, dosage):
    total_proteins = proteins.shape[1]
    groups = lax.axis_size("protein")
    block_width = total_proteins // groups
    column = lax.axis_index("protein")
    sample_count = proteins.shape[0] * lax.axis_size("sample")
    contract = (((0,), (0,)), ((), ()))
    own_proteins = lax.dynamic_slice_in_dim(proteins, column * block_width, block_width, 1)
    gram_part = lax.dot_general(
        proteins, own_proteins, contract, preferred_element_type=jnp.float32
    )
    cross_part = lax.dot_general(dosage, own_proteins, contract, preferred_element_type=jnp.float32)
    protein_sums = jnp.sum(own_proteins, axis=0, dtype=jnp.float32)
    dose_sums = jnp.sum(dosage, axis=0, dtype=jnp.float32)
    dose_squares = jnp.sum(dosage * dosage, axis=0, dtype=jnp.float32)
    gram_total, protein_sums = lax.psum((gram_part, protein_sums), "sample")
    cross, dose_sums, dose_squares = side_by_side(
        (cross_part, dose_sums, dose_squares), "sample", 0, 1
    )
    gram_cols = gram_total / sample_count
    gram = lax.all_gather(gram_cols, "protein", axis=1, tiled=True)
    means = dose_sums / sample_count
    spread = jnp.sqrt(dose_squares / sample_count - means * means + 1e-05)
    centred = (cross - means[:, None] * protein_sums[None, :]) / (
        spread[:, None] * math.sqrt(sample_count)
    )
    centred_rows = lax.all_gather(centred, "protein", axis=1, tiled=True)
    scores_rows = factor_solve(gram, centred_rows)
    return lax.dynamic_slice_in_dim(scores_rows, column * block_width, block_width, 1)


def solution(mesh):
    in_specs = (P("sample", None), P("sample", None))
    out_specs = P("sample", "protein")
    return jax.shard_map(body, mesh=mesh, in_specs=in_specs, out_specs=out_specs, check_vma=False)
```

```python
import functools
import math

import jax
import jax.numpy as jnp
from jax import lax
from jax.experimental import pallas as pl
from jax.experimental.pallas import tpu as pltpu
from jax.sharding import PartitionSpec as P

BLOCK = 128
CHUNK = 256
HIGHEST = lax.Precision.HIGHEST


def side_by_side(arrays, axis, dim, along):
    widths = [math.prod(a.shape[along:]) for a in arrays]
    both = jnp.concatenate(
        [a.reshape(*a.shape[:along], w) for a, w in zip(arrays, widths)], axis=along
    )
    filled = lax.psum_scatter(both, axis, scatter_dimension=dim, tiled=True)
    tiles = jnp.split(filled, [sum(widths[:k]) for k in range(1, len(widths))], axis=along)
    return tuple(
        (b.reshape(*filled.shape[:along], *a.shape[along:]) for a, b in zip(arrays, tiles))
    )


def dot_t(a, b):
    return lax.dot_general(
        a, b, (((1,), (1,)), ((), ())), precision=HIGHEST, preferred_element_type=jnp.float32
    )


def inverse_factor(block):
    b = block.shape[0]
    sub = lax.broadcasted_iota(jnp.int32, (8, b), 0)
    lane = lax.broadcasted_iota(jnp.int32, (8, b), 1)
    lane_row = lax.broadcasted_iota(jnp.int32, (1, b), 1)
    tiles = [block[r : r + 8, :] for r in range(0, b, 8)]
    for j in range(b):
        home, t = divmod(j, 8)
        row = tiles[home][t : t + 1, :]
        scale = lax.rsqrt(row[:, j : j + 1])
        new_row = jnp.where(lane_row == j, scale, row * scale)
        for r in range(home, len(tiles)):
            tile = tiles[r]
            mult = tile[:, j : j + 1] * scale
            hit = lane == j
            if r == home:
                mult = jnp.where(sub[:, 0:1] > t, mult, 0.0)
                hit = hit & (sub > t)
            tile = jnp.where(hit, 0.0, tile) - mult * new_row
            if r == home:
                tile = jnp.where(sub == t, jnp.where(lane_row <= j, new_row, 0.0), tile)
            tiles[r] = tile
    return jnp.concatenate(tiles, axis=0)


def factor_solve_kernel(g_hbm, c_ref, out_ref, g_ref, sem):
    n = g_ref.shape[0]
    b = BLOCK
    copy = pltpu.make_async_copy(g_hbm, g_ref, sem)
    copy.start()
    out_ref[...] = c_ref[...]
    copy.wait()
    for k in range(n // b):
        r0 = k * b
        inv = inverse_factor(g_ref[r0 : r0 + b, r0 : r0 + b])
        solved = dot_t(out_ref[:, r0 : r0 + b], inv)
        out_ref[:, r0 : r0 + b] = solved
        rest = r0 + b
        if rest < n:
            panel = dot_t(g_ref[rest:, r0 : r0 + b], inv)
            for a in range(rest, n, CHUNK):
                e = min(a + CHUNK, n)
                g_ref[a:e, rest:] = g_ref[a:e, rest:] - dot_t(panel[a - rest : e - rest], panel)
            out_ref[:, rest:] = out_ref[:, rest:] - dot_t(solved, panel)


def factor_solve(gram, rows):
    n = gram.shape[0]
    return pl.pallas_call(
        factor_solve_kernel,
        out_shape=jax.ShapeDtypeStruct(rows.shape, jnp.float32),
        in_specs=[
            pl.BlockSpec(memory_space=pl.ANY),
            pl.BlockSpec(memory_space=pltpu.VMEM),
        ],
        out_specs=pl.BlockSpec(memory_space=pltpu.VMEM),
        scratch_shapes=[
            pltpu.VMEM((n, n), jnp.float32),
            pltpu.SemaphoreType.DMA,
        ],
        compiler_params=pltpu.CompilerParams(vmem_limit_bytes=56 * 1024 * 1024),
    )(gram, rows)


def body(proteins, dosage):
    total_proteins = proteins.shape[1]
    groups = lax.axis_size("protein")
    block_width = total_proteins // groups
    column = lax.axis_index("protein")
    sample_count = proteins.shape[0] * lax.axis_size("sample")
    contract = (((0,), (0,)), ((), ()))
    own_proteins = lax.dynamic_slice_in_dim(proteins, column * block_width, block_width, 1)
    gram_part = lax.dot_general(
        proteins, own_proteins, contract, preferred_element_type=jnp.float32
    )
    cross_part = lax.dot_general(dosage, own_proteins, contract, preferred_element_type=jnp.float32)
    protein_sums = jnp.sum(own_proteins, axis=0, dtype=jnp.float32)
    dose_sums = jnp.sum(dosage, axis=0, dtype=jnp.float32)
    dose_squares = jnp.sum(dosage * dosage, axis=0, dtype=jnp.float32)
    gram_total, protein_sums = lax.psum((gram_part, protein_sums), "sample")
    cross, dose_sums, dose_squares = side_by_side(
        (cross_part, dose_sums, dose_squares), "sample", 0, 1
    )
    gram_cols = gram_total / sample_count
    gram = lax.all_gather(gram_cols, "protein", axis=1, tiled=True)
    means = dose_sums / sample_count
    spread = jnp.sqrt(dose_squares / sample_count - means * means + 1e-05)
    centred = (cross - means[:, None] * protein_sums[None, :]) / (
        spread[:, None] * math.sqrt(sample_count)
    )
    centred_rows = lax.all_gather(centred, "protein", axis=1, tiled=True)
    scores_rows = factor_solve(gram, centred_rows)
    return lax.dynamic_slice_in_dim(scores_rows, column * block_width, block_width, 1)


def solution(mesh):
    in_specs = (P("sample", None), P("sample", None))
    out_specs = P("sample", "protein")
    return jax.shard_map(body, mesh=mesh, in_specs=in_specs, out_specs=out_specs, check_vma=False)
```

```python
import math

import jax
import jax.numpy as jnp
from jax import lax
from jax.experimental import pallas as pl
from jax.experimental.pallas import tpu as pltpu
from jax.sharding import PartitionSpec as P

BLOCK = 128
CHUNK = 256
HIGHEST = lax.Precision.HIGHEST


def side_by_side(arrays, axis, dim, along):
    widths = [math.prod(a.shape[along:]) for a in arrays]
    both = jnp.concatenate(
        [a.reshape(*a.shape[:along], w) for a, w in zip(arrays, widths)], axis=along
    )
    filled = lax.psum_scatter(both, axis, scatter_dimension=dim, tiled=True)
    tiles = jnp.split(filled, [sum(widths[:k]) for k in range(1, len(widths))], axis=along)
    return tuple(
        (b.reshape(*filled.shape[:along], *a.shape[along:]) for a, b in zip(arrays, tiles))
    )


def dot_t(a, b):
    return lax.dot_general(
        a, b, (((1,), (1,)), ((), ())), precision=HIGHEST, preferred_element_type=jnp.float32
    )


def inverse_factor(block):
    b = block.shape[0]
    sub = lax.broadcasted_iota(jnp.int32, (8, b), 0)
    lane = lax.broadcasted_iota(jnp.int32, (8, b), 1)
    lane_row = lax.broadcasted_iota(jnp.int32, (1, b), 1)
    tiles = [block[r : r + 8, :] for r in range(0, b, 8)]
    for j in range(b):
        home, t = divmod(j, 8)
        row = tiles[home][t : t + 1, :]
        scale = lax.rsqrt(row[:, j : j + 1])
        new_row = jnp.where(lane_row == j, scale, row * scale)
        for r in range(home, len(tiles)):
            tile = tiles[r]
            mult = tile[:, j : j + 1] * scale
            hit = lane == j
            if r == home:
                mult = jnp.where(sub[:, 0:1] > t, mult, 0.0)
                hit = hit & (sub > t)
            tile = jnp.where(hit, 0.0, tile) - mult * new_row
            if r == home:
                tile = jnp.where(sub == t, jnp.where(lane_row <= j, new_row, 0.0), tile)
            tiles[r] = tile
    return jnp.concatenate(tiles, axis=0)


def factor_kernel(g_hbm, l_hbm, g_ref, sem):
    n = g_ref.shape[0]
    b = BLOCK
    copy = pltpu.make_async_copy(g_hbm, g_ref, sem)
    copy.start()
    copy.wait()
    for k in range(n // b):
        r0 = k * b
        inv = inverse_factor(g_ref[r0 : r0 + b, r0 : r0 + b])
        g_ref[r0 : r0 + b, r0 : r0 + b] = inv
        rest = r0 + b
        if rest < n:
            panel = dot_t(g_ref[rest:, r0 : r0 + b], inv)
            g_ref[rest:, r0 : r0 + b] = panel
            for a in range(rest, n, CHUNK):
                e = min(a + CHUNK, n)
                g_ref[a:e, rest:] = g_ref[a:e, rest:] - dot_t(panel[a - rest : e - rest], panel)
    copy = pltpu.make_async_copy(g_ref, l_hbm, sem)
    copy.start()
    copy.wait()


def solve_kernel(l_hbm, c_ref, out_ref, l_ref, sem):
    n = l_ref.shape[0]
    b = BLOCK
    copy = pltpu.make_async_copy(l_hbm, l_ref, sem)
    copy.start()
    out_ref[...] = c_ref[...]
    copy.wait()
    for k in range(n // b):
        r0 = k * b
        solved = dot_t(out_ref[:, r0 : r0 + b], l_ref[r0 : r0 + b, r0 : r0 + b])
        out_ref[:, r0 : r0 + b] = solved
        rest = r0 + b
        if rest < n:
            out_ref[:, rest:] = out_ref[:, rest:] - dot_t(solved, l_ref[rest:, r0 : r0 + b])


def factor(gram):
    n = gram.shape[0]
    return pl.pallas_call(
        factor_kernel,
        out_shape=jax.ShapeDtypeStruct(gram.shape, jnp.float32),
        in_specs=[pl.BlockSpec(memory_space=pl.ANY)],
        out_specs=pl.BlockSpec(memory_space=pl.ANY),
        scratch_shapes=[pltpu.VMEM((n, n), jnp.float32), pltpu.SemaphoreType.DMA],
        input_output_aliases={0: 0},
        compiler_params=pltpu.CompilerParams(vmem_limit_bytes=56 * 1024 * 1024),
    )(gram)


def solve(factored, rows):
    n = factored.shape[0]
    return pl.pallas_call(
        solve_kernel,
        out_shape=jax.ShapeDtypeStruct(rows.shape, jnp.float32),
        in_specs=[
            pl.BlockSpec(memory_space=pl.ANY),
            pl.BlockSpec(memory_space=pltpu.VMEM),
        ],
        out_specs=pl.BlockSpec(memory_space=pltpu.VMEM),
        scratch_shapes=[pltpu.VMEM((n, n), jnp.float32), pltpu.SemaphoreType.DMA],
        compiler_params=pltpu.CompilerParams(vmem_limit_bytes=40 * 1024 * 1024),
    )(factored, rows)


def body(proteins, dosage):
    total_proteins = proteins.shape[1]
    groups = lax.axis_size("protein")
    block_width = total_proteins // groups
    column = lax.axis_index("protein")
    sample_count = proteins.shape[0] * lax.axis_size("sample")
    contract = (((0,), (0,)), ((), ()))
    own_proteins = lax.dynamic_slice_in_dim(proteins, column * block_width, block_width, 1)
    gram_part = lax.dot_general(
        proteins, own_proteins, contract, preferred_element_type=jnp.float32
    )
    cross_part = lax.dot_general(dosage, own_proteins, contract, preferred_element_type=jnp.float32)
    protein_sums = jnp.sum(own_proteins, axis=0, dtype=jnp.float32)
    dose_sums = jnp.sum(dosage, axis=0, dtype=jnp.float32)
    dose_squares = jnp.sum(dosage * dosage, axis=0, dtype=jnp.float32)
    stacked = jnp.concatenate(
        [gram_part, protein_sums[None, :], jnp.zeros((7, block_width), jnp.float32)], axis=0
    )
    stacked = lax.psum(stacked, "sample")
    gram_cols = stacked[:total_proteins] / sample_count
    protein_sums = stacked[total_proteins]
    gram = lax.all_gather(gram_cols, "protein", axis=1, tiled=True)
    gram, cross_part, dose_sums, dose_squares = lax.optimization_barrier(
        (gram, cross_part, dose_sums, dose_squares)
    )
    factored = factor(gram)
    cross, dose_sums, dose_squares = side_by_side(
        (cross_part, dose_sums, dose_squares), "sample", 0, 1
    )
    means = dose_sums / sample_count
    spread = jnp.sqrt(dose_squares / sample_count - means * means + 1e-05)
    centred = (cross - means[:, None] * protein_sums[None, :]) / (
        spread[:, None] * math.sqrt(sample_count)
    )
    centred_rows = lax.all_gather(centred, "protein", axis=1, tiled=True)
    scores_rows = solve(factored, centred_rows)
    return lax.dynamic_slice_in_dim(scores_rows, column * block_width, block_width, 1)


def solution(mesh):
    in_specs = (P("sample", None), P("sample", None))
    out_specs = P("sample", "protein")
    return jax.shard_map(body, mesh=mesh, in_specs=in_specs, out_specs=out_specs, check_vma=False)
```

```python
import math

import jax
import jax.numpy as jnp
from jax import lax
from jax.experimental import pallas as pl
from jax.experimental.pallas import tpu as pltpu
from jax.sharding import PartitionSpec as P

BLOCK = 128
PIECE = 256
HIGHEST = lax.Precision.HIGHEST


def side_by_side(arrays, axis, dim, along):
    widths = [math.prod(a.shape[along:]) for a in arrays]
    both = jnp.concatenate(
        [a.reshape(*a.shape[:along], w) for a, w in zip(arrays, widths)], axis=along
    )
    filled = lax.psum_scatter(both, axis, scatter_dimension=dim, tiled=True)
    tiles = jnp.split(filled, [sum(widths[:k]) for k in range(1, len(widths))], axis=along)
    return tuple(
        (b.reshape(*filled.shape[:along], *a.shape[along:]) for a, b in zip(arrays, tiles))
    )


def dot_t(a, b):
    return lax.dot_general(
        a, b, (((1,), (1,)), ((), ())), precision=HIGHEST, preferred_element_type=jnp.float32
    )


def inverse_factor(block):
    b = block.shape[0]
    sub = lax.broadcasted_iota(jnp.int32, (8, b), 0)
    lane = lax.broadcasted_iota(jnp.int32, (8, b), 1)
    lane_row = lax.broadcasted_iota(jnp.int32, (1, b), 1)
    tiles = [block[r : r + 8, :] for r in range(0, b, 8)]
    for j in range(b):
        home, t = divmod(j, 8)
        row = tiles[home][t : t + 1, :]
        scale = lax.rsqrt(row[:, j : j + 1])
        new_row = jnp.where(lane_row == j, scale, row * scale)
        for r in range(home, len(tiles)):
            tile = tiles[r]
            mult = tile[:, j : j + 1] * scale
            hit = lane == j
            if r == home:
                mult = jnp.where(sub[:, 0:1] > t, mult, 0.0)
                hit = hit & (sub > t)
            tile = jnp.where(hit, 0.0, tile) - mult * new_row
            if r == home:
                tile = jnp.where(sub == t, jnp.where(lane_row <= j, new_row, 0.0), tile)
            tiles[r] = tile
    return jnp.concatenate(tiles, axis=0)


def lower_blocks(n, groups):
    count = n // PIECE
    blocks = [(i, j) for i in range(count) for j in range(i + 1)]
    assert len(blocks) % groups == 0
    return blocks


def factor_kernel(packed_hbm, l_hbm, g_ref, sems):
    n = g_ref.shape[0]
    b = BLOCK
    blocks = lower_blocks(n, 1)
    copies = []
    for q, (i, j) in enumerate(blocks):
        copy = pltpu.make_async_copy(
            packed_hbm.at[q],
            g_ref.at[pl.ds(i * PIECE, PIECE), pl.ds(j * PIECE, PIECE)],
            sems.at[q],
        )
        copy.start()
        copies.append(copy)
    for copy in copies:
        copy.wait()
    for k in range(n // b):
        r0 = k * b
        inv = inverse_factor(g_ref[r0 : r0 + b, r0 : r0 + b])
        g_ref[r0 : r0 + b, r0 : r0 + b] = inv
        rest = r0 + b
        if rest < n:
            panel = dot_t(g_ref[rest:, r0 : r0 + b], inv)
            g_ref[rest:, r0 : r0 + b] = panel
            edges = sorted(set([rest] + list(range(-(-rest // PIECE) * PIECE, n, PIECE)) + [n]))
            for a, e in zip(edges[:-1], edges[1:]):
                g_ref[a:e, rest:e] = g_ref[a:e, rest:e] - dot_t(
                    panel[a - rest : e - rest], panel[: e - rest]
                )
    copy = pltpu.make_async_copy(g_ref, l_hbm, sems.at[0])
    copy.start()
    copy.wait()


def solve_kernel(l_hbm, c_ref, out_ref, l_ref, sem):
    n = l_ref.shape[0]
    b = BLOCK
    copy = pltpu.make_async_copy(l_hbm, l_ref, sem)
    copy.start()
    out_ref[...] = c_ref[...]
    copy.wait()
    for k in range(n // b):
        r0 = k * b
        solved = dot_t(out_ref[:, r0 : r0 + b], l_ref[r0 : r0 + b, r0 : r0 + b])
        out_ref[:, r0 : r0 + b] = solved
        rest = r0 + b
        if rest < n:
            out_ref[:, rest:] = out_ref[:, rest:] - dot_t(solved, l_ref[rest:, r0 : r0 + b])


def factor(packed, n):
    return pl.pallas_call(
        factor_kernel,
        out_shape=jax.ShapeDtypeStruct((n, n), jnp.float32),
        in_specs=[pl.BlockSpec(memory_space=pl.ANY)],
        out_specs=pl.BlockSpec(memory_space=pl.ANY),
        scratch_shapes=[
            pltpu.VMEM((n, n), jnp.float32),
            pltpu.SemaphoreType.DMA((packed.shape[0],)),
        ],
        compiler_params=pltpu.CompilerParams(vmem_limit_bytes=56 * 1024 * 1024),
    )(packed)


def solve(factored, rows):
    n = factored.shape[0]
    return pl.pallas_call(
        solve_kernel,
        out_shape=jax.ShapeDtypeStruct(rows.shape, jnp.float32),
        in_specs=[
            pl.BlockSpec(memory_space=pl.ANY),
            pl.BlockSpec(memory_space=pltpu.VMEM),
        ],
        out_specs=pl.BlockSpec(memory_space=pltpu.VMEM),
        scratch_shapes=[pltpu.VMEM((n, n), jnp.float32), pltpu.SemaphoreType.DMA],
        compiler_params=pltpu.CompilerParams(vmem_limit_bytes=40 * 1024 * 1024),
    )(factored, rows)


def body(proteins, dosage):
    total_proteins = proteins.shape[1]
    groups = lax.axis_size("protein")
    block_width = total_proteins // groups
    column = lax.axis_index("protein")
    sample_count = proteins.shape[0] * lax.axis_size("sample")
    contract = (((0,), (0,)), ((), ()))
    own_proteins = lax.dynamic_slice_in_dim(proteins, column * block_width, block_width, 1)
    blocks = lower_blocks(total_proteins, groups)
    share = len(blocks) // groups
    table = jnp.asarray([[blocks[z * share + t] for t in range(share)] for z in range(groups)], jnp.int32)
    mine = table[column]
    pieces = proteins.reshape(proteins.shape[0], total_proteins // PIECE, PIECE)
    left = jnp.take(pieces, mine[:, 0], axis=1)
    right = jnp.take(pieces, mine[:, 1], axis=1)
    gram_part = lax.dot_general(
        left, right, (((0,), (0,)), ((1,), (1,))), preferred_element_type=jnp.float32
    )
    cross_part = lax.dot_general(dosage, own_proteins, contract, preferred_element_type=jnp.float32)
    protein_sums = jnp.sum(own_proteins, axis=0, dtype=jnp.float32)
    dose_sums = jnp.sum(dosage, axis=0, dtype=jnp.float32)
    dose_squares = jnp.sum(dosage * dosage, axis=0, dtype=jnp.float32)
    stacked = jnp.concatenate([gram_part.reshape(-1), protein_sums])
    stacked = lax.psum(stacked, "sample")
    gram_own = stacked[: gram_part.size].reshape(gram_part.shape) / sample_count
    protein_sums = stacked[gram_part.size :]
    packed = lax.all_gather(gram_own, "protein", axis=0, tiled=True)
    packed, cross_part, dose_sums, dose_squares = lax.optimization_barrier(
        (packed, cross_part, dose_sums, dose_squares)
    )
    factored = factor(packed, total_proteins)
    cross, dose_sums, dose_squares = side_by_side(
        (cross_part, dose_sums, dose_squares), "sample", 0, 1
    )
    means = dose_sums / sample_count
    spread = jnp.sqrt(dose_squares / sample_count - means * means + 1e-05)
    centred = (cross - means[:, None] * protein_sums[None, :]) / (
        spread[:, None] * math.sqrt(sample_count)
    )
    centred_rows = lax.all_gather(centred, "protein", axis=1, tiled=True)
    scores_rows = solve(factored, centred_rows)
    return lax.dynamic_slice_in_dim(scores_rows, column * block_width, block_width, 1)


def solution(mesh):
    in_specs = (P("sample", None), P("sample", None))
    out_specs = P("sample", "protein")
    return jax.shard_map(body, mesh=mesh, in_specs=in_specs, out_specs=out_specs, check_vma=False)
```

```python
import math

import jax
import jax.numpy as jnp
from jax import lax
from jax.experimental import pallas as pl
from jax.experimental.pallas import tpu as pltpu
from jax.sharding import PartitionSpec as P

BLOCK = 128
PIECE = 256
HIGHEST = lax.Precision.HIGHEST


def side_by_side(arrays, axis, dim, along):
    widths = [math.prod(a.shape[along:]) for a in arrays]
    both = jnp.concatenate(
        [a.reshape(*a.shape[:along], w) for a, w in zip(arrays, widths)], axis=along
    )
    filled = lax.psum_scatter(both, axis, scatter_dimension=dim, tiled=True)
    tiles = jnp.split(filled, [sum(widths[:k]) for k in range(1, len(widths))], axis=along)
    return tuple(
        (b.reshape(*filled.shape[:along], *a.shape[along:]) for a, b in zip(arrays, tiles))
    )


def dot_t(a, b):
    return lax.dot_general(
        a, b, (((1,), (1,)), ((), ())), precision=HIGHEST, preferred_element_type=jnp.float32
    )


def inverse_factor(block):
    b = block.shape[0]
    sub = lax.broadcasted_iota(jnp.int32, (8, b), 0)
    lane = lax.broadcasted_iota(jnp.int32, (8, b), 1)
    lane_row = lax.broadcasted_iota(jnp.int32, (1, b), 1)
    tiles = [block[r : r + 8, :] for r in range(0, b, 8)]
    for j in range(b):
        home, t = divmod(j, 8)
        row = tiles[home][t : t + 1, :]
        scale = lax.rsqrt(row[:, j : j + 1])
        new_row = jnp.where(lane_row == j, scale, row * scale)
        for r in range(home, len(tiles)):
            tile = tiles[r]
            mult = tile[:, j : j + 1] * scale
            hit = lane == j
            if r == home:
                mult = jnp.where(sub[:, 0:1] > t, mult, 0.0)
                hit = hit & (sub > t)
            tile = jnp.where(hit, 0.0, tile) - mult * new_row
            if r == home:
                tile = jnp.where(sub == t, jnp.where(lane_row <= j, new_row, 0.0), tile)
            tiles[r] = tile
    return jnp.concatenate(tiles, axis=0)


def lower_blocks(n, groups):
    count = n // PIECE
    blocks = [(i, j) for i in range(count) for j in range(i + 1)]
    assert len(blocks) % groups == 0
    return blocks


def factor_kernel(packed_hbm, l_hbm, g_ref, sems):
    n = g_ref.shape[0]
    b = BLOCK
    blocks = lower_blocks(n, 1)
    copies = []
    for q, (i, j) in enumerate(blocks):
        copy = pltpu.make_async_copy(
            packed_hbm.at[q],
            g_ref.at[pl.ds(i * PIECE, PIECE), pl.ds(j * PIECE, PIECE)],
            sems.at[q],
        )
        copy.start()
        copies.append(copy)
    for copy in copies:
        copy.wait()
    for k in range(n // b):
        r0 = k * b
        inv = inverse_factor(g_ref[r0 : r0 + b, r0 : r0 + b])
        g_ref[r0 : r0 + b, r0 : r0 + b] = inv
        rest = r0 + b
        if rest < n:
            panel = dot_t(g_ref[rest:, r0 : r0 + b], inv)
            g_ref[rest:, r0 : r0 + b] = panel
            edges = sorted(set([rest] + list(range(-(-rest // PIECE) * PIECE, n, PIECE)) + [n]))
            for a, e in zip(edges[:-1], edges[1:]):
                g_ref[a:e, rest:e] = g_ref[a:e, rest:e] - dot_t(
                    panel[a - rest : e - rest], panel[: e - rest]
                )
    copy = pltpu.make_async_copy(g_ref, l_hbm, sems.at[0])
    copy.start()
    copy.wait()


def solve_kernel(l_hbm, c_ref, out_ref, l_ref, sem):
    n = l_ref.shape[0]
    b = BLOCK
    copy = pltpu.make_async_copy(l_hbm, l_ref, sem)
    copy.start()
    width = c_ref.shape[2]
    for z in range(c_ref.shape[0]):
        out_ref[:, z * width : (z + 1) * width] = c_ref[z]
    copy.wait()
    for k in range(n // b):
        r0 = k * b
        solved = dot_t(out_ref[:, r0 : r0 + b], l_ref[r0 : r0 + b, r0 : r0 + b])
        out_ref[:, r0 : r0 + b] = solved
        rest = r0 + b
        if rest < n:
            out_ref[:, rest:] = out_ref[:, rest:] - dot_t(solved, l_ref[rest:, r0 : r0 + b])


def factor(packed, n):
    return pl.pallas_call(
        factor_kernel,
        out_shape=jax.ShapeDtypeStruct((n, n), jnp.float32),
        in_specs=[pl.BlockSpec(memory_space=pl.ANY)],
        out_specs=pl.BlockSpec(memory_space=pl.ANY),
        scratch_shapes=[
            pltpu.VMEM((n, n), jnp.float32),
            pltpu.SemaphoreType.DMA((packed.shape[0],)),
        ],
        compiler_params=pltpu.CompilerParams(vmem_limit_bytes=56 * 1024 * 1024),
    )(packed)


def solve(factored, rows):
    n = factored.shape[0]
    return pl.pallas_call(
        solve_kernel,
        out_shape=jax.ShapeDtypeStruct((rows.shape[1], n), jnp.float32),
        in_specs=[
            pl.BlockSpec(memory_space=pl.ANY),
            pl.BlockSpec(memory_space=pltpu.VMEM),
        ],
        out_specs=pl.BlockSpec(memory_space=pltpu.VMEM),
        scratch_shapes=[pltpu.VMEM((n, n), jnp.float32), pltpu.SemaphoreType.DMA],
        compiler_params=pltpu.CompilerParams(vmem_limit_bytes=40 * 1024 * 1024),
    )(factored, rows)


def body(proteins, dosage):
    total_proteins = proteins.shape[1]
    groups = lax.axis_size("protein")
    block_width = total_proteins // groups
    column = lax.axis_index("protein")
    sample_count = proteins.shape[0] * lax.axis_size("sample")
    contract = (((0,), (0,)), ((), ()))
    own_proteins = lax.dynamic_slice_in_dim(proteins, column * block_width, block_width, 1)
    blocks = lower_blocks(total_proteins, groups)
    share = len(blocks) // groups
    table = jnp.asarray([[blocks[z * share + t] for t in range(share)] for z in range(groups)], jnp.int32)
    mine = table[column]
    pieces = proteins.reshape(proteins.shape[0], total_proteins // PIECE, PIECE)
    left = jnp.take(pieces, mine[:, 0], axis=1)
    right = jnp.take(pieces, mine[:, 1], axis=1)
    gram_part = lax.dot_general(
        left, right, (((0,), (0,)), ((1,), (1,))), preferred_element_type=jnp.float32
    )
    cross_part = lax.dot_general(dosage, own_proteins, contract, preferred_element_type=jnp.float32)
    protein_sums = jnp.sum(own_proteins, axis=0, dtype=jnp.float32)
    dose_sums = jnp.sum(dosage, axis=0, dtype=jnp.float32)
    dose_squares = jnp.sum(dosage * dosage, axis=0, dtype=jnp.float32)
    stacked = jnp.concatenate([gram_part.reshape(-1), protein_sums])
    stacked = lax.psum(stacked, "sample")
    gram_own = stacked[: gram_part.size].reshape(gram_part.shape) / sample_count
    protein_sums = stacked[gram_part.size :]
    packed = lax.all_gather(gram_own, "protein", axis=0, tiled=True)
    packed, cross_part, dose_sums, dose_squares = lax.optimization_barrier(
        (packed, cross_part, dose_sums, dose_squares)
    )
    factored = factor(packed, total_proteins)
    cross, dose_sums, dose_squares = side_by_side(
        (cross_part, dose_sums, dose_squares), "sample", 0, 1
    )
    means = dose_sums / sample_count
    spread = jnp.sqrt(dose_squares / sample_count - means * means + 1e-05)
    centred = (cross - means[:, None] * protein_sums[None, :]) / (
        spread[:, None] * math.sqrt(sample_count)
    )
    centred_rows = lax.all_gather(centred, "protein", axis=0)
    scores_rows = solve(factored, centred_rows)
    return lax.dynamic_slice_in_dim(scores_rows, column * block_width, block_width, 1)


def solution(mesh):
    in_specs = (P("sample", None), P("sample", None))
    out_specs = P("sample", "protein")
    return jax.shard_map(body, mesh=mesh, in_specs=in_specs, out_specs=out_specs, check_vma=False)
```

```python
import math

import jax
import jax.numpy as jnp
from jax import lax
from jax.experimental import pallas as pl
from jax.experimental.pallas import tpu as pltpu
from jax.sharding import PartitionSpec as P

BLOCK = 128
PIECE = 256
HIGHEST = lax.Precision.HIGHEST


def side_by_side(arrays, axis, dim, along):
    widths = [math.prod(a.shape[along:]) for a in arrays]
    both = jnp.concatenate(
        [a.reshape(*a.shape[:along], w) for a, w in zip(arrays, widths)], axis=along
    )
    filled = lax.psum_scatter(both, axis, scatter_dimension=dim, tiled=True)
    tiles = jnp.split(filled, [sum(widths[:k]) for k in range(1, len(widths))], axis=along)
    return tuple(
        (b.reshape(*filled.shape[:along], *a.shape[along:]) for a, b in zip(arrays, tiles))
    )


def dot_t(a, b):
    return lax.dot_general(
        a, b, (((1,), (1,)), ((), ())), precision=HIGHEST, preferred_element_type=jnp.float32
    )


def inverse_factor(block):
    b = block.shape[0]
    sub = lax.broadcasted_iota(jnp.int32, (8, b), 0)
    lane = lax.broadcasted_iota(jnp.int32, (8, b), 1)
    lane_row = lax.broadcasted_iota(jnp.int32, (1, b), 1)
    tiles = [block[r : r + 8, :] for r in range(0, b, 8)]
    for j in range(b):
        home, t = divmod(j, 8)
        row = tiles[home][t : t + 1, :]
        scale = lax.rsqrt(row[:, j : j + 1])
        new_row = jnp.where(lane_row == j, scale, row * scale)
        for r in range(home, len(tiles)):
            tile = tiles[r]
            mult = tile[:, j : j + 1] * scale
            hit = lane == j
            if r == home:
                mult = jnp.where(sub[:, 0:1] > t, mult, 0.0)
                hit = hit & (sub > t)
            tile = jnp.where(hit, 0.0, tile) - mult * new_row
            if r == home:
                tile = jnp.where(sub == t, jnp.where(lane_row <= j, new_row, 0.0), tile)
            tiles[r] = tile
    return jnp.concatenate(tiles, axis=0)


def lower_blocks(n, groups):
    count = n // PIECE
    blocks = [(i, j) for i in range(count) for j in range(i + 1)]
    assert len(blocks) % groups == 0
    return blocks


def factor_kernel(packed_hbm, l_hbm, g_ref, sems):
    n = g_ref.shape[0]
    b = BLOCK
    blocks = lower_blocks(n, 1)
    copies = []
    for q, (i, j) in enumerate(blocks):
        copy = pltpu.make_async_copy(
            packed_hbm.at[q],
            g_ref.at[pl.ds(i * PIECE, PIECE), pl.ds(j * PIECE, PIECE)],
            sems.at[q],
        )
        copy.start()
        copies.append(copy)
    copies[0].wait()
    first = inverse_factor(g_ref[0:b, 0:b])
    for copy in copies[1:]:
        copy.wait()
    for k in range(n // b):
        r0 = k * b
        inv = first if k == 0 else inverse_factor(g_ref[r0 : r0 + b, r0 : r0 + b])
        g_ref[r0 : r0 + b, r0 : r0 + b] = inv
        rest = r0 + b
        if rest < n:
            panel = dot_t(g_ref[rest:, r0 : r0 + b], inv)
            g_ref[rest:, r0 : r0 + b] = panel
            edges = sorted(set([rest] + list(range(-(-rest // PIECE) * PIECE, n, PIECE)) + [n]))
            for a, e in zip(edges[:-1], edges[1:]):
                g_ref[a:e, rest:e] = g_ref[a:e, rest:e] - dot_t(
                    panel[a - rest : e - rest], panel[: e - rest]
                )
    copy = pltpu.make_async_copy(g_ref, l_hbm, sems.at[0])
    copy.start()
    copy.wait()


def solve_kernel(l_hbm, c_ref, out_ref, l_ref, sem):
    n = l_ref.shape[0]
    b = BLOCK
    copy = pltpu.make_async_copy(l_hbm, l_ref, sem)
    copy.start()
    out_ref[...] = c_ref[...]
    copy.wait()
    for k in range(n // b):
        r0 = k * b
        solved = dot_t(out_ref[:, r0 : r0 + b], l_ref[r0 : r0 + b, r0 : r0 + b])
        out_ref[:, r0 : r0 + b] = solved
        rest = r0 + b
        if rest < n:
            out_ref[:, rest:] = out_ref[:, rest:] - dot_t(solved, l_ref[rest:, r0 : r0 + b])


def factor(packed, n):
    return pl.pallas_call(
        factor_kernel,
        out_shape=jax.ShapeDtypeStruct((n, n), jnp.float32),
        in_specs=[pl.BlockSpec(memory_space=pl.ANY)],
        out_specs=pl.BlockSpec(memory_space=pl.ANY),
        scratch_shapes=[
            pltpu.VMEM((n, n), jnp.float32),
            pltpu.SemaphoreType.DMA((packed.shape[0],)),
        ],
        compiler_params=pltpu.CompilerParams(vmem_limit_bytes=56 * 1024 * 1024),
    )(packed)


def solve(factored, rows):
    n = factored.shape[0]
    return pl.pallas_call(
        solve_kernel,
        out_shape=jax.ShapeDtypeStruct(rows.shape, jnp.float32),
        in_specs=[
            pl.BlockSpec(memory_space=pl.ANY),
            pl.BlockSpec(memory_space=pltpu.VMEM),
        ],
        out_specs=pl.BlockSpec(memory_space=pltpu.VMEM),
        scratch_shapes=[pltpu.VMEM((n, n), jnp.float32), pltpu.SemaphoreType.DMA],
        compiler_params=pltpu.CompilerParams(vmem_limit_bytes=40 * 1024 * 1024),
    )(factored, rows)


def body(proteins, dosage):
    total_proteins = proteins.shape[1]
    groups = lax.axis_size("protein")
    block_width = total_proteins // groups
    column = lax.axis_index("protein")
    sample_count = proteins.shape[0] * lax.axis_size("sample")
    contract = (((0,), (0,)), ((), ()))
    own_proteins = lax.dynamic_slice_in_dim(proteins, column * block_width, block_width, 1)
    blocks = lower_blocks(total_proteins, groups)
    share = len(blocks) // groups
    table = jnp.asarray([[blocks[z * share + t] for t in range(share)] for z in range(groups)], jnp.int32)
    mine = table[column]
    pieces = proteins.reshape(proteins.shape[0], total_proteins // PIECE, PIECE)
    left = jnp.take(pieces, mine[:, 0], axis=1)
    right = jnp.take(pieces, mine[:, 1], axis=1)
    gram_part = lax.dot_general(
        left, right, (((0,), (0,)), ((1,), (1,))), preferred_element_type=jnp.float32
    )
    cross_part = lax.dot_general(dosage, own_proteins, contract, preferred_element_type=jnp.float32)
    protein_sums = jnp.sum(own_proteins, axis=0, dtype=jnp.float32)
    dose_sums = jnp.sum(dosage, axis=0, dtype=jnp.float32)
    dose_squares = jnp.sum(dosage * dosage, axis=0, dtype=jnp.float32)
    stacked = jnp.concatenate([gram_part.reshape(-1), protein_sums])
    stacked = lax.psum(stacked, "sample")
    gram_own = stacked[: gram_part.size].reshape(gram_part.shape) / sample_count
    protein_sums = stacked[gram_part.size :]
    packed = lax.all_gather(gram_own, "protein", axis=0, tiled=True)
    packed, cross_part, dose_sums, dose_squares = lax.optimization_barrier(
        (packed, cross_part, dose_sums, dose_squares)
    )
    factored = factor(packed, total_proteins)
    cross, dose_sums, dose_squares = side_by_side(
        (cross_part, dose_sums, dose_squares), "sample", 0, 1
    )
    means = dose_sums / sample_count
    spread = jnp.sqrt(dose_squares / sample_count - means * means + 1e-05)
    centred = (cross - means[:, None] * protein_sums[None, :]) / (
        spread[:, None] * math.sqrt(sample_count)
    )
    centred_rows = lax.all_gather(centred, "protein", axis=1, tiled=True)
    scores_rows = solve(factored, centred_rows)
    return lax.dynamic_slice_in_dim(scores_rows, column * block_width, block_width, 1)


def solution(mesh):
    in_specs = (P("sample", None), P("sample", None))
    out_specs = P("sample", "protein")
    return jax.shard_map(body, mesh=mesh, in_specs=in_specs, out_specs=out_specs, check_vma=False)
```
